256 devices in a mesh: dp: 4 (over x), feat: 8 (over y, core), cent: 8 (over z).
Axes of the slice: x: 4, y: 4, z: 8, core: 2. Of those that a mesh axis runs over, the one named last changes fastest.
Arguments:
- embeddings: bfloat16 [8192, 768], P(('dp', 'cent')), may hold values from -12 to 12
- projection: bfloat16 [768, 8192], P(None, 'feat'), may hold values from -0.21875 to 0.21875
- phases: float32 [8192], P('feat'), may hold values from -4 to 4
- centroids: bfloat16 [4096, 8192], P('cent', 'feat'), may hold values from -7 to 7
Outputs:
- updated: float32 [4096, 8192], P('cent', 'feat')
The draws below stay inside these ranges and needn't reach their ends.
All inputs are finite; a program needn't handle non-finite values.
Results may differ from the reference program's by a relative error of at most 0.0003.
Values may be sent and summed in bfloat16 or wider, within the bound.
No kernel may reach another device: no remote copies, remote signals or barrier semaphores. Data moves between devices by JAX's collectives and lax.ppermute only.
A program may use at most 64 MiB of HBM per device.

```python
import math
import jax
import jax.numpy as jnp
from jax import lax

E = 768
F = 8192
K = 4096
ROWS = 8192


def phase_values(key):
    return jax.random.uniform(jax.random.fold_in(key, 17), (F,), jnp.float32, -math.pi, math.pi)


def draw_phases(key, part):
    return phase_values(key)


def draw_embeddings(key, part):
    raw_normal = jax.random.normal(jax.random.fold_in(key, 23), (ROWS, E), jnp.float32)
    values = jnp.clip(raw_normal, -6.0, 6.0)
    return values.astype(jnp.bfloat16)


def draw_centroids(key, part):
    values = jnp.clip(jax.random.normal(jax.random.fold_in(key, 29), (K, F), jnp.float32), -6.0, 6.0)
    return values.astype(jnp.bfloat16)


def block_scale(stream_key, shape, split, low, largest):
    loudness = 1.0
    for position, shards_of in split:
        heights = jax.random.uniform(jax.random.fold_in(jax.random.fold_in(stream_key, 6), position), (shards_of,), jnp.float32, low / len(split), largest / len(split))
        loudness = loudness * jnp.repeat(jnp.exp(heights), shape[position] // shards_of).reshape((-1,) + (1,) * (len(shape) - 1 - position))
    return loudness


def scatter_about(key, extent, deviation, limit, pieces=(), kind=jnp.bfloat16):
    result = jax.random.normal(key, extent, jnp.float32) * deviation
    if len(pieces) > 0:
        result = block_scale(key, extent, pieces, -0.22, 0.18) * result
    return jnp.clip(result, min=-limit, max=limit).astype(kind)


def setup_inputs(seed: int = 0) -> dict:
    arg_keys = jax.random.split(jax.random.key(seed), 5)
    embeddings = draw_embeddings(jax.random.fold_in(arg_keys[4], 71), 0)
    projection = scatter_about(arg_keys[1], (E, F), E ** -0.5, 0.21875, ((1, 8),))
    phases = draw_phases(jax.random.fold_in(arg_keys[4], 71), 0)
    centroids = draw_centroids(jax.random.fold_in(arg_keys[4], 71), 0)
    return {"embeddings": embeddings, "projection": projection, "phases": phases, "centroids": centroids}


SQRT_TWO = math.sqrt(2.0)
SHARP_FACTOR = 1.5
PRIOR_MASS = 1.0

def reference(embeddings, projection, phases, centroids):
    projected = jnp.dot(embeddings, projection, preferred_element_type=jnp.float32)
    features = (SQRT_TWO * jnp.cos(projected + phases)).astype(jnp.bfloat16)
    center_wide = centroids.astype(jnp.float32)
    center_sq = lax.optimization_barrier(jnp.sum(center_wide * center_wide, axis=1))
    inner_prod = jnp.dot(features, centroids.T, preferred_element_type=jnp.float32)
    sharpness = SHARP_FACTOR / math.sqrt(F)
    logits = sharpness * (2.0 * inner_prod - center_sq[None, :])
    top_score = lax.optimization_barrier(jnp.max(logits, axis=1, keepdims=True))
    exp_terms = jnp.exp(logits - top_score)
    resp = (exp_terms / lax.optimization_barrier(jnp.sum(exp_terms, axis=1, keepdims=True))).astype(jnp.bfloat16)
    mass = lax.optimization_barrier(jnp.sum(resp.astype(jnp.float32), axis=0))
    sums = jnp.dot(resp.T, features, preferred_element_type=jnp.float32)
    return (sums + PRIOR_MASS * center_wide) / (mass + PRIOR_MASS)[:, None]
```

```python
import math

import jax
import jax.numpy as jnp
from jax import lax
from jax.sharding import PartitionSpec as P

F = 8192


SQRT_TWO = math.sqrt(2.0)
SHARP_FACTOR = 1.5
PRIOR_MASS = 1.0


def featurize(embeddings, projection, phases):
    projected = jnp.dot(embeddings, projection, preferred_element_type=jnp.float32)
    return (SQRT_TWO * jnp.cos(projected + phases)).astype(jnp.bfloat16)


def shards(embeddings, projection, phases, centroids):
    features = featurize(embeddings, projection, phases)
    group_features = lax.all_gather(features, "cent", axis=0, tiled=True)
    sharpness = SHARP_FACTOR / math.sqrt(F)

    center_wide = centroids.astype(jnp.float32)
    center_sq = jnp.sum(center_wide * center_wide, axis=1)
    inner_part = lax.dot_general(
        group_features, centroids, (((1,), (1,)), ((), ())), preferred_element_type=jnp.float32
    )
    partial_value = 2.0 * inner_part - center_sq[None, :]
    logits = sharpness * lax.psum_scatter(partial_value, "feat", scatter_dimension=0, tiled=True)

    local_top = jnp.max(logits, axis=1)
    local_sum = jnp.sum(jnp.exp(logits - local_top[:, None]), axis=1)
    stats = lax.all_gather(jnp.stack([local_top, local_sum]), "cent", axis=0)
    top_score = jnp.max(stats[:, 0], axis=0)
    total = jnp.sum(stats[:, 1] * jnp.exp(stats[:, 0] - top_score[None, :]), axis=0)
    resp = (jnp.exp(logits - top_score[:, None]) / total[:, None]).astype(jnp.bfloat16)

    group_resp = lax.all_gather(resp, "feat", axis=0, tiled=True)
    mass_part = jnp.sum(group_resp.astype(jnp.float32), axis=0)
    sums_part = lax.dot_general(
        group_resp, group_features, (((0,), (0,)), ((), ())), preferred_element_type=jnp.float32
    )
    width = sums_part.shape[1]
    mass_rows = -(-mass_part.shape[0] // width)
    mass_block = jnp.pad(mass_part, (0, mass_rows * width - mass_part.shape[0])).reshape(mass_rows, width)
    both = lax.psum(jnp.concatenate([sums_part, mass_block], axis=0), "dp")
    sums = both[: sums_part.shape[0]]
    mass = both[sums_part.shape[0] :].reshape(-1)[: mass_part.shape[0]]
    return (sums + PRIOR_MASS * center_wide) / (mass + PRIOR_MASS)[:, None]


def solution(mesh):
    return jax.shard_map(
        shards,
        mesh=mesh,
        in_specs=(P(("dp", "cent"), None), P(None, "feat"), P("feat"), P("cent", "feat")),
        out_specs=P("cent", "feat"),
        check_vma=False,
    )
```

```python
import math

import jax
import jax.numpy as jnp
from jax import lax
from jax.sharding import PartitionSpec as P

F = 8192


SQRT_TWO = math.sqrt(2.0)
SHARP_FACTOR = 1.5
PRIOR_MASS = 1.0


def featurize(embeddings, projection, phases):
    projected = jnp.dot(embeddings, projection, preferred_element_type=jnp.float32)
    return (SQRT_TWO * jnp.cos(projected + phases)).astype(jnp.bfloat16)


def shards(embeddings, projection, phases, centroids):
    features = featurize(embeddings, projection, phases)
    group_features = lax.all_gather(features, "cent", axis=0, tiled=True)
    sharpness = SHARP_FACTOR / math.sqrt(F)

    center_wide = centroids.astype(jnp.float32)
    center_sq = jnp.sum(center_wide * center_wide, axis=1)
    inner_part = lax.dot_general(
        group_features, centroids, (((1,), (1,)), ((), ())), preferred_element_type=jnp.float32
    )
    partial_value = 2.0 * inner_part - center_sq[None, :]
    logits = sharpness * lax.psum_scatter(partial_value, "feat", scatter_dimension=0, tiled=True)

    local_top = jnp.max(logits, axis=1)
    local_sum = jnp.sum(jnp.exp(logits - local_top[:, None]), axis=1)
    pair = jnp.stack([local_top, local_sum])
    n_cent = lax.axis_size("cent")
    received = [pair]
    for shift in range(1, n_cent):
        received.append(lax.ppermute(pair, "cent", [(i, (i + shift) % n_cent) for i in range(n_cent)]))
    stats = jnp.stack(received)
    top_score = jnp.max(stats[:, 0], axis=0)
    total = jnp.sum(stats[:, 1] * jnp.exp(stats[:, 0] - top_score[None, :]), axis=0)
    resp = (jnp.exp(logits - top_score[:, None]) / total[:, None]).astype(jnp.bfloat16)

    group_resp = lax.all_gather(resp, "feat", axis=0, tiled=True)
    mass_part = jnp.sum(group_resp.astype(jnp.float32), axis=0)
    sums_part = lax.dot_general(
        group_resp, group_features, (((0,), (0,)), ((), ())), preferred_element_type=jnp.float32
    )
    width = sums_part.shape[1]
    mass_rows = -(-mass_part.shape[0] // width)
    mass_block = jnp.pad(mass_part, (0, mass_rows * width - mass_part.shape[0])).reshape(mass_rows, width)
    both = lax.psum(jnp.concatenate([sums_part, mass_block], axis=0), "dp")
    sums = both[: sums_part.shape[0]]
    mass = both[sums_part.shape[0] :].reshape(-1)[: mass_part.shape[0]]
    return (sums + PRIOR_MASS * center_wide) / (mass + PRIOR_MASS)[:, None]


def solution(mesh):
    return jax.shard_map(
        shards,
        mesh=mesh,
        in_specs=(P(("dp", "cent"), None), P(None, "feat"), P("feat"), P("cent", "feat")),
        out_specs=P("cent", "feat"),
        check_vma=False,
    )
```

```python
import math

import jax
import jax.numpy as jnp
from jax import lax
from jax.sharding import PartitionSpec as P

F = 8192


SQRT_TWO = math.sqrt(2.0)
SHARP_FACTOR = 1.5
PRIOR_MASS = 1.0


def featurize(embeddings, projection, phases):
    projected = jnp.dot(embeddings, projection, preferred_element_type=jnp.float32)
    return (SQRT_TWO * jnp.cos(projected + phases)).astype(jnp.bfloat16)


def shards(embeddings, projection, phases, centroids):
    features = featurize(embeddings, projection, phases)
    group_features = lax.all_gather(features, "cent", axis=0, tiled=True)
    sharpness = SHARP_FACTOR / math.sqrt(F)

    center_wide = centroids.astype(jnp.float32)
    center_sq = jnp.sum(center_wide * center_wide, axis=1)
    inner_part = lax.dot_general(
        group_features, centroids, (((1,), (1,)), ((), ())), preferred_element_type=jnp.float32
    )
    partial_value = 2.0 * inner_part - center_sq[None, :]
    on_chip = lax.psum_scatter(partial_value, "feat_core", scatter_dimension=0, tiled=True)
    logits = sharpness * lax.psum_scatter(on_chip, "feat_chip", scatter_dimension=0, tiled=True)

    local_top = jnp.max(logits, axis=1)
    local_sum = jnp.sum(jnp.exp(logits - local_top[:, None]), axis=1)
    pair = jnp.stack([local_top, local_sum])
    n_cent = lax.axis_size("cent")
    received = [pair]
    for shift in range(1, n_cent):
        received.append(lax.ppermute(pair, "cent", [(i, (i + shift) % n_cent) for i in range(n_cent)]))
    stats = jnp.stack(received)
    top_score = jnp.max(stats[:, 0], axis=0)
    total = jnp.sum(stats[:, 1] * jnp.exp(stats[:, 0] - top_score[None, :]), axis=0)
    resp = (jnp.exp(logits - top_score[:, None]) / total[:, None]).astype(jnp.bfloat16)

    chip_resp = lax.all_gather(resp, "feat_chip", axis=0, tiled=True)
    group_resp = lax.all_gather(chip_resp, "feat_core", axis=0, tiled=True)
    mass_part = jnp.sum(group_resp.astype(jnp.float32), axis=0)
    sums_part = lax.dot_general(
        group_resp, group_features, (((0,), (0,)), ((), ())), preferred_element_type=jnp.float32
    )
    width = sums_part.shape[1]
    mass_rows = -(-mass_part.shape[0] // width)
    mass_block = jnp.pad(mass_part, (0, mass_rows * width - mass_part.shape[0])).reshape(mass_rows, width)
    both = lax.psum(jnp.concatenate([sums_part, mass_block], axis=0), "dp")
    sums = both[: sums_part.shape[0]]
    mass = both[sums_part.shape[0] :].reshape(-1)[: mass_part.shape[0]]
    return (sums + PRIOR_MASS * center_wide) / (mass + PRIOR_MASS)[:, None]


def solution(mesh):
    n_dp, n_feat, n_cent = (mesh.shape[a] for a in ("dp", "feat", "cent"))
    split = jax.sharding.Mesh(
        mesh.devices.reshape(n_dp, n_feat // 2, 2, n_cent), ("dp", "feat_chip", "feat_core", "cent")
    )
    feat = ("feat_chip", "feat_core")
    return jax.shard_map(
        shards,
        mesh=split,
        in_specs=(P(("dp", "cent"), None), P(None, feat), P(feat), P("cent", feat)),
        out_specs=P("cent", feat),
        check_vma=False,
    )
```

```python
import math

import jax
import jax.numpy as jnp
from jax import lax
from jax.sharding import PartitionSpec as P

F = 8192


SQRT_TWO = math.sqrt(2.0)
SHARP_FACTOR = 1.5
PRIOR_MASS = 1.0


def featurize(embeddings, projection, phases):
    projected = jnp.dot(embeddings, projection, preferred_element_type=jnp.float32)
    return (SQRT_TWO * jnp.cos(projected + phases)).astype(jnp.bfloat16)


def shards(embeddings, projection, phases, centroids):
    features = featurize(embeddings, projection, phases)
    group_features = lax.all_gather(features, "cent", axis=0, tiled=True)
    sharpness = SHARP_FACTOR / math.sqrt(F)

    center_wide = centroids.astype(jnp.float32)
    center_sq = jnp.sum(center_wide * center_wide, axis=1)
    inner_part = lax.dot_general(
        group_features, centroids, (((1,), (1,)), ((), ())), preferred_element_type=jnp.float32
    )
    partial_value = 2.0 * inner_part - center_sq[None, :]
    logits = sharpness * lax.psum_scatter(partial_value, "feat", scatter_dimension=0, tiled=True)

    local_top = jnp.max(logits, axis=1)
    local_sum = jnp.sum(jnp.exp(logits - local_top[:, None]), axis=1)
    pair = jnp.stack([local_top, local_sum])
    n_cent = lax.axis_size("cent")
    received = [pair]
    for shift in range(1, n_cent):
        received.append(lax.ppermute(pair, "cent", [(i, (i + shift) % n_cent) for i in range(n_cent)]))
    stats = jnp.stack(received)
    top_score = jnp.max(stats[:, 0], axis=0)
    total = jnp.sum(stats[:, 1] * jnp.exp(stats[:, 0] - top_score[None, :]), axis=0)
    resp = (jnp.exp(logits - top_score[:, None]) / total[:, None]).astype(jnp.bfloat16)

    group_resp = lax.all_gather(resp, "feat", axis=0, tiled=True)
    mass_part = jnp.sum(group_resp.astype(jnp.float32), axis=0)
    sums_part = lax.dot_general(
        group_resp, group_features, (((0,), (0,)), ((), ())), preferred_element_type=jnp.float32
    )
    n_dp = lax.axis_size("dp")
    me = lax.axis_index("dp")
    n_rows, width = sums_part.shape
    split = n_rows // 2
    chunk = (n_rows - split) // n_dp

    def as_rows(values):
        count = -(-values.shape[-1] // width)
        padded = jnp.pad(values, [(0, 0)] * (values.ndim - 1) + [(0, count * width - values.shape[-1])])
        return padded.reshape(values.shape[:-1] + (count, width))

    both = lax.psum(jnp.concatenate([sums_part[:split], as_rows(mass_part[:split])], axis=0), "dp")
    mass = both[split:].reshape(-1)[:split]

    pieces = jnp.concatenate(
        [sums_part[split:].reshape(n_dp, chunk, width), as_rows(mass_part[split:].reshape(n_dp, chunk))], axis=1
    )
    owned = lax.dynamic_index_in_dim(pieces, me, 0, keepdims=False)
    for shift in range(1, n_dp):
        ring = [(i, (i + shift) % n_dp) for i in range(n_dp)]
        outgoing = lax.dynamic_index_in_dim(pieces, (me + shift) % n_dp, 0, keepdims=False)
        owned = owned + lax.ppermute(outgoing, "dp", ring)
    old_owned = lax.dynamic_slice_in_dim(center_wide, split + me * chunk, chunk, 0)
    mass_owned = owned[chunk:].reshape(-1)[:chunk]
    fresh = (owned[:chunk] + PRIOR_MASS * old_owned) / (mass_owned + PRIOR_MASS)[:, None]
    arrived = [fresh]
    for shift in range(1, n_dp):
        ring = [(i, (i + shift) % n_dp) for i in range(n_dp)]
        arrived.append(lax.ppermute(fresh, "dp", ring))
    order = (me - jnp.arange(n_dp)) % n_dp
    lower = jnp.take(jnp.stack(arrived), order, axis=0).reshape(n_rows - split, width)

    upper = (both[:split] + PRIOR_MASS * center_wide[:split]) / (mass + PRIOR_MASS)[:, None]
    return jnp.concatenate([upper, lower], axis=0)


def solution(mesh):
    return jax.shard_map(
        shards,
        mesh=mesh,
        in_specs=(P(("dp", "cent"), None), P(None, "feat"), P("feat"), P("cent", "feat")),
        out_specs=P("cent", "feat"),
        check_vma=False,
    )
```

```python
import math

import jax
import jax.numpy as jnp
from jax import lax
from jax.sharding import PartitionSpec as P

F = 8192


SQRT_TWO = math.sqrt(2.0)
SHARP_FACTOR = 1.5
PRIOR_MASS = 1.0


def featurize(embeddings, projection, phases):
    projected = jnp.dot(embeddings, projection, preferred_element_type=jnp.float32)
    return (SQRT_TWO * jnp.cos(projected + phases)).astype(jnp.bfloat16)


def shards(embeddings, projection, phases, centroids):
    features = featurize(embeddings, projection, phases)
    group_features = lax.all_gather(features, "cent", axis=0, tiled=True)
    sharpness = SHARP_FACTOR / math.sqrt(F)

    center_wide = centroids.astype(jnp.float32)
    center_sq = jnp.sum(center_wide * center_wide, axis=1)
    inner_part = lax.dot_general(
        group_features, centroids, (((1,), (1,)), ((), ())), preferred_element_type=jnp.float32
    )
    partial_value = 2.0 * inner_part - center_sq[None, :]
    logits = sharpness * lax.psum_scatter(partial_value, "feat", scatter_dimension=0, tiled=True)

    local_top = jnp.max(logits, axis=1)
    local_sum = jnp.sum(jnp.exp(logits - local_top[:, None]), axis=1)
    pair = jnp.stack([local_top, local_sum])
    n_cent = lax.axis_size("cent")
    received = [pair]
    for shift in range(1, n_cent):
        received.append(lax.ppermute(pair, "cent", [(i, (i + shift) % n_cent) for i in range(n_cent)]))
    stats = jnp.stack(received)
    top_score = jnp.max(stats[:, 0], axis=0)
    total = jnp.sum(stats[:, 1] * jnp.exp(stats[:, 0] - top_score[None, :]), axis=0)
    resp = (jnp.exp(logits - top_score[:, None]) / total[:, None]).astype(jnp.bfloat16)

    group_resp = lax.all_gather(resp, "feat", axis=0, tiled=True)
    mass_part = jnp.sum(group_resp.astype(jnp.float32), axis=0)
    n_rows = group_resp.shape[1]
    split = n_rows // 4
    width = group_features.shape[1]

    def row_contract(weights):
        return lax.dot_general(
            weights, group_features, (((0,), (0,)), ((), ())), preferred_element_type=jnp.float32
        )
    n_dp = lax.axis_size("dp")
    me = lax.axis_index("dp")
    chunk = (n_rows - split) // n_dp

    def as_rows(values):
        count = -(-values.shape[-1] // width)
        padded = jnp.pad(values, [(0, 0)] * (values.ndim - 1) + [(0, count * width - values.shape[-1])])
        return padded.reshape(values.shape[:-1] + (count, width))

    both = lax.psum(jnp.concatenate([row_contract(group_resp[:, :split]), as_rows(mass_part[:split])], axis=0), "dp")
    mass = both[split:].reshape(-1)[:split]

    pieces = jnp.concatenate(
        [row_contract(group_resp[:, split:]).reshape(n_dp, chunk, width), as_rows(mass_part[split:].reshape(n_dp, chunk))], axis=1
    )
    owned = lax.dynamic_index_in_dim(pieces, me, 0, keepdims=False)
    for shift in range(1, n_dp):
        ring = [(i, (i + shift) % n_dp) for i in range(n_dp)]
        outgoing = lax.dynamic_index_in_dim(pieces, (me + shift) % n_dp, 0, keepdims=False)
        owned = owned + lax.ppermute(outgoing, "dp", ring)
    old_owned = lax.dynamic_slice_in_dim(center_wide, split + me * chunk, chunk, 0)
    mass_owned = owned[chunk:].reshape(-1)[:chunk]
    fresh = (owned[:chunk] + PRIOR_MASS * old_owned) / (mass_owned + PRIOR_MASS)[:, None]
    arrived = [fresh]
    for shift in range(1, n_dp):
        ring = [(i, (i + shift) % n_dp) for i in range(n_dp)]
        arrived.append(lax.ppermute(fresh, "dp", ring))
    order = (me - jnp.arange(n_dp)) % n_dp
    lower = jnp.take(jnp.stack(arrived), order, axis=0).reshape(n_rows - split, width)

    upper = (both[:split] + PRIOR_MASS * center_wide[:split]) / (mass + PRIOR_MASS)[:, None]
    return jnp.concatenate([upper, lower], axis=0)


def solution(mesh):
    return jax.shard_map(
        shards,
        mesh=mesh,
        in_specs=(P(("dp", "cent"), None), P(None, "feat"), P("feat"), P("cent", "feat")),
        out_specs=P("cent", "feat"),
        check_vma=False,
    )
```

```python
import math

import jax
import jax.numpy as jnp
from jax import lax
from jax.sharding import PartitionSpec as P

F = 8192


SQRT_TWO = math.sqrt(2.0)
SHARP_FACTOR = 1.5
PRIOR_MASS = 1.0


def featurize(embeddings, projection, phases):
    projected = jnp.dot(embeddings, projection, preferred_element_type=jnp.float32)
    return (SQRT_TWO * jnp.cos(projected + phases)).astype(jnp.bfloat16)


def shards(embeddings, projection, phases, centroids):
    features = featurize(embeddings, projection, phases)
    group_features = lax.all_gather(features, "cent", axis=0, tiled=True)
    sharpness = SHARP_FACTOR / math.sqrt(F)

    center_wide = centroids.astype(jnp.float32)
    center_sq = jnp.sum(center_wide * center_wide, axis=1)
    inner_part = lax.dot_general(
        group_features, centroids, (((1,), (1,)), ((), ())), preferred_element_type=jnp.float32
    )
    partial_value = 2.0 * inner_part - center_sq[None, :]
    logits = sharpness * lax.psum_scatter(partial_value, "feat", scatter_dimension=0, tiled=True)

    local_top = jnp.max(logits, axis=1)
    local_sum = jnp.sum(jnp.exp(logits - local_top[:, None]), axis=1)
    pair = jnp.stack([local_top, local_sum])
    n_cent = lax.axis_size("cent")
    received = [pair]
    for shift in range(1, n_cent):
        received.append(lax.ppermute(pair, "cent", [(i, (i + shift) % n_cent) for i in range(n_cent)]))
    stats = jnp.stack(received)
    top_score = jnp.max(stats[:, 0], axis=0)
    total = jnp.sum(stats[:, 1] * jnp.exp(stats[:, 0] - top_score[None, :]), axis=0)
    resp = (jnp.exp(logits - top_score[:, None]) / total[:, None]).astype(jnp.bfloat16)

    group_resp = lax.all_gather(resp, "feat", axis=0, tiled=True)
    n_rows = group_resp.shape[1]
    split = 3 * n_rows // 8
    width = group_features.shape[1]

    def row_contract(weights):
        return lax.dot_general(
            weights, group_features, (((0,), (0,)), ((), ())), preferred_element_type=jnp.float32
        )

    def as_rows(values):
        count = -(-values.shape[-1] // width)
        padded = jnp.pad(values, [(0, 0)] * (values.ndim - 1) + [(0, count * width - values.shape[-1])])
        return padded.reshape(values.shape[:-1] + (count, width))

    n_dp = lax.axis_size("dp")
    me = lax.axis_index("dp")
    chunk = (n_rows - split) // n_dp
    head_resp = group_resp[:, :split]
    head = jnp.concatenate(
        [row_contract(head_resp), as_rows(jnp.sum(head_resp.astype(jnp.float32), axis=0))], axis=0
    )
    head, tail_resp = lax.optimization_barrier((head, group_resp[:, split:]))
    both = lax.psum(head, "dp")
    mass = both[split:].reshape(-1)[:split]

    tail_mass = jnp.sum(tail_resp.astype(jnp.float32), axis=0)
    pieces = jnp.concatenate(
        [row_contract(tail_resp).reshape(n_dp, chunk, width), as_rows(tail_mass.reshape(n_dp, chunk))], axis=1
    )
    owned = lax.dynamic_index_in_dim(pieces, me, 0, keepdims=False)
    for shift in range(1, n_dp):
        ring = [(i, (i + shift) % n_dp) for i in range(n_dp)]
        outgoing = lax.dynamic_index_in_dim(pieces, (me + shift) % n_dp, 0, keepdims=False)
        owned = owned + lax.ppermute(outgoing, "dp", ring)
    old_owned = lax.dynamic_slice_in_dim(center_wide, split + me * chunk, chunk, 0)
    mass_owned = owned[chunk:].reshape(-1)[:chunk]
    fresh = (owned[:chunk] + PRIOR_MASS * old_owned) / (mass_owned + PRIOR_MASS)[:, None]
    arrived = [fresh]
    for shift in range(1, n_dp):
        ring = [(i, (i + shift) % n_dp) for i in range(n_dp)]
        arrived.append(lax.ppermute(fresh, "dp", ring))
    order = (me - jnp.arange(n_dp)) % n_dp
    lower = jnp.take(jnp.stack(arrived), order, axis=0).reshape(n_rows - split, width)

    upper = (both[:split] + PRIOR_MASS * center_wide[:split]) / (mass + PRIOR_MASS)[:, None]
    return jnp.concatenate([upper, lower], axis=0)


def solution(mesh):
    return jax.shard_map(
        shards,
        mesh=mesh,
        in_specs=(P(("dp", "cent"), None), P(None, "feat"), P("feat"), P("cent", "feat")),
        out_specs=P("cent", "feat"),
        check_vma=False,
    )
```

```python
import math

import jax
import jax.numpy as jnp
from jax import lax
from jax.sharding import PartitionSpec as P

F = 8192


SQRT_TWO = math.sqrt(2.0)
SHARP_FACTOR = 1.5
PRIOR_MASS = 1.0


def featurize(embeddings, projection, phases):
    projected = jnp.dot(embeddings, projection, preferred_element_type=jnp.float32)
    return (SQRT_TWO * jnp.cos(projected + phases)).astype(jnp.bfloat16)


def shards(embeddings, projection, phases, centroids):
    features = featurize(embeddings, projection, phases)
    n_cent = lax.axis_size("cent")
    me_cent = lax.axis_index("cent")
    half = features.shape[1] // 2
    by_sc = lax.all_gather(features[:, :half], "cent", axis=0, tiled=True)
    own = features[:, half:]
    to_right = [(i, (i + 1) % n_cent) for i in range(n_cent)]
    to_left = [(i, (i - 1) % n_cent) for i in range(n_cent)]
    from_left, from_right = [own], []
    moving_right, moving_left = own, own
    for step in range(1, n_cent // 2 + 1):
        moving_right = lax.ppermute(moving_right, "cent", to_right)
        from_left.append(moving_right)
        if step < n_cent - step:
            moving_left = lax.ppermute(moving_left, "cent", to_left)
            from_right.append(moving_left)
    arrived = jnp.stack(from_left + from_right[::-1])
    order = (me_cent - jnp.arange(n_cent)) % n_cent
    by_ring = jnp.take(arrived, order, axis=0).reshape(-1, own.shape[1])
    group_features = jnp.concatenate([by_sc, by_ring], axis=1)
    sharpness = SHARP_FACTOR / math.sqrt(F)

    center_wide = centroids.astype(jnp.float32)
    center_sq = jnp.sum(center_wide * center_wide, axis=1)
    inner_part = lax.dot_general(
        group_features, centroids, (((1,), (1,)), ((), ())), preferred_element_type=jnp.float32
    )
    partial_value = 2.0 * inner_part - center_sq[None, :]
    logits = sharpness * lax.psum_scatter(partial_value, "feat", scatter_dimension=0, tiled=True)

    local_top = jnp.max(logits, axis=1)
    local_sum = jnp.sum(jnp.exp(logits - local_top[:, None]), axis=1)
    pair = jnp.stack([local_top, local_sum])
    received = [pair]
    for shift in range(1, n_cent):
        received.append(lax.ppermute(pair, "cent", [(i, (i + shift) % n_cent) for i in range(n_cent)]))
    stats = jnp.stack(received)
    top_score = jnp.max(stats[:, 0], axis=0)
    total = jnp.sum(stats[:, 1] * jnp.exp(stats[:, 0] - top_score[None, :]), axis=0)
    resp = (jnp.exp(logits - top_score[:, None]) / total[:, None]).astype(jnp.bfloat16)

    group_resp = lax.all_gather(resp, "feat", axis=0, tiled=True)
    mass_part = jnp.sum(group_resp.astype(jnp.float32), axis=0)
    n_rows = group_resp.shape[1]
    split = n_rows // 4
    width = group_features.shape[1]

    def row_contract(weights):
        return lax.dot_general(
            weights, group_features, (((0,), (0,)), ((), ())), preferred_element_type=jnp.float32
        )
    n_dp = lax.axis_size("dp")
    me = lax.axis_index("dp")
    chunk = (n_rows - split) // n_dp

    def as_rows(values):
        count = -(-values.shape[-1] // width)
        padded = jnp.pad(values, [(0, 0)] * (values.ndim - 1) + [(0, count * width - values.shape[-1])])
        return padded.reshape(values.shape[:-1] + (count, width))

    both = lax.psum(jnp.concatenate([row_contract(group_resp[:, :split]), as_rows(mass_part[:split])], axis=0), "dp")
    mass = both[split:].reshape(-1)[:split]

    pieces = jnp.concatenate(
        [row_contract(group_resp[:, split:]).reshape(n_dp, chunk, width), as_rows(mass_part[split:].reshape(n_dp, chunk))], axis=1
    )
    owned = lax.dynamic_index_in_dim(pieces, me, 0, keepdims=False)
    for shift in range(1, n_dp):
        ring = [(i, (i + shift) % n_dp) for i in range(n_dp)]
        outgoing = lax.dynamic_index_in_dim(pieces, (me + shift) % n_dp, 0, keepdims=False)
        owned = owned + lax.ppermute(outgoing, "dp", ring)
    old_owned = lax.dynamic_slice_in_dim(center_wide, split + me * chunk, chunk, 0)
    mass_owned = owned[chunk:].reshape(-1)[:chunk]
    fresh = (owned[:chunk] + PRIOR_MASS * old_owned) / (mass_owned + PRIOR_MASS)[:, None]
    arrived = [fresh]
    for shift in range(1, n_dp):
        ring = [(i, (i + shift) % n_dp) for i in range(n_dp)]
        arrived.append(lax.ppermute(fresh, "dp", ring))
    order = (me - jnp.arange(n_dp)) % n_dp
    lower = jnp.take(jnp.stack(arrived), order, axis=0).reshape(n_rows - split, width)

    upper = (both[:split] + PRIOR_MASS * center_wide[:split]) / (mass + PRIOR_MASS)[:, None]
    return jnp.concatenate([upper, lower], axis=0)


def solution(mesh):
    return jax.shard_map(
        shards,
        mesh=mesh,
        in_specs=(P(("dp", "cent"), None), P(None, "feat"), P("feat"), P("cent", "feat")),
        out_specs=P("cent", "feat"),
        check_vma=False,
    )
```

```python
import math

import jax
import jax.numpy as jnp
from jax import lax
from jax.sharding import PartitionSpec as P

F = 8192


SQRT_TWO = math.sqrt(2.0)
SHARP_FACTOR = 1.5
PRIOR_MASS = 1.0


def featurize(embeddings, projection, phases):
    projected = jnp.dot(embeddings, projection, preferred_element_type=jnp.float32)
    return (SQRT_TWO * jnp.cos(projected + phases)).astype(jnp.bfloat16)


def shards(embeddings, projection, phases, centroids):
    features = featurize(embeddings, projection, phases)
    group_features = lax.all_gather(features, "cent", axis=0, tiled=True)
    sharpness = SHARP_FACTOR / math.sqrt(F)

    center_wide = centroids.astype(jnp.float32)
    center_sq = jnp.sum(center_wide * center_wide, axis=1)
    inner_part = lax.dot_general(
        group_features, centroids, (((1,), (1,)), ((), ())), preferred_element_type=jnp.float32
    )
    partial_value = 2.0 * inner_part - center_sq[None, :]
    logits = sharpness * lax.psum_scatter(partial_value, "feat", scatter_dimension=0, tiled=True)

    local_top = jnp.max(logits, axis=1)
    local_sum = jnp.sum(jnp.exp(logits - local_top[:, None]), axis=1)
    n_cent = lax.axis_size("cent")
    top_score, total = local_top, local_sum
    if n_cent & (n_cent - 1) == 0:
        bit = 1
        while bit < n_cent:
            pair = lax.ppermute(
                jnp.stack([top_score, total]), "cent", [(i, i ^ bit) for i in range(n_cent)]
            )
            merged = jnp.maximum(top_score, pair[0])
            total = total * jnp.exp(top_score - merged) + pair[1] * jnp.exp(pair[0] - merged)
            top_score = merged
            bit *= 2
    else:
        pair = jnp.stack([local_top, local_sum])
        received = [pair]
        for shift in range(1, n_cent):
            received.append(lax.ppermute(pair, "cent", [(i, (i + shift) % n_cent) for i in range(n_cent)]))
        stats = jnp.stack(received)
        top_score = jnp.max(stats[:, 0], axis=0)
        total = jnp.sum(stats[:, 1] * jnp.exp(stats[:, 0] - top_score[None, :]), axis=0)
    resp = (jnp.exp(logits - top_score[:, None]) / total[:, None]).astype(jnp.bfloat16)

    group_resp = lax.all_gather(resp, "feat", axis=0, tiled=True)
    mass_part = jnp.sum(group_resp.astype(jnp.float32), axis=0)
    n_rows = group_resp.shape[1]
    split = n_rows // 4
    width = group_features.shape[1]

    def row_contract(weights):
        return lax.dot_general(
            weights, group_features, (((0,), (0,)), ((), ())), preferred_element_type=jnp.float32
        )
    n_dp = lax.axis_size("dp")
    me = lax.axis_index("dp")
    chunk = (n_rows - split) // n_dp

    def as_rows(values):
        count = -(-values.shape[-1] // width)
        padded = jnp.pad(values, [(0, 0)] * (values.ndim - 1) + [(0, count * width - values.shape[-1])])
        return padded.reshape(values.shape[:-1] + (count, width))

    both = lax.psum(jnp.concatenate([row_contract(group_resp[:, :split]), as_rows(mass_part[:split])], axis=0), "dp")
    mass = both[split:].reshape(-1)[:split]

    pieces = jnp.concatenate(
        [row_contract(group_resp[:, split:]).reshape(n_dp, chunk, width), as_rows(mass_part[split:].reshape(n_dp, chunk))], axis=1
    )
    owned = lax.dynamic_index_in_dim(pieces, me, 0, keepdims=False)
    for shift in range(1, n_dp):
        ring = [(i, (i + shift) % n_dp) for i in range(n_dp)]
        outgoing = lax.dynamic_index_in_dim(pieces, (me + shift) % n_dp, 0, keepdims=False)
        owned = owned + lax.ppermute(outgoing, "dp", ring)
    old_owned = lax.dynamic_slice_in_dim(center_wide, split + me * chunk, chunk, 0)
    mass_owned = owned[chunk:].reshape(-1)[:chunk]
    fresh = (owned[:chunk] + PRIOR_MASS * old_owned) / (mass_owned + PRIOR_MASS)[:, None]
    arrived = [fresh]
    for shift in range(1, n_dp):
        ring = [(i, (i + shift) % n_dp) for i in range(n_dp)]
        arrived.append(lax.ppermute(fresh, "dp", ring))
    order = (me - jnp.arange(n_dp)) % n_dp
    lower = jnp.take(jnp.stack(arrived), order, axis=0).reshape(n_rows - split, width)

    upper = (both[:split] + PRIOR_MASS * center_wide[:split]) / (mass + PRIOR_MASS)[:, None]
    return jnp.concatenate([upper, lower], axis=0)


def solution(mesh):
    return jax.shard_map(
        shards,
        mesh=mesh,
        in_specs=(P(("dp", "cent"), None), P(None, "feat"), P("feat"), P("cent", "feat")),
        out_specs=P("cent", "feat"),
        check_vma=False,
    )
```

```python
import math

import jax
import jax.numpy as jnp
from jax import lax
from jax.sharding import PartitionSpec as P

F = 8192


SQRT_TWO = math.sqrt(2.0)
SHARP_FACTOR = 1.5
PRIOR_MASS = 1.0


def featurize(embeddings, projection, phases):
    projected = jnp.dot(embeddings, projection, preferred_element_type=jnp.float32)
    return (SQRT_TWO * jnp.cos(projected + phases)).astype(jnp.bfloat16)


def shards(embeddings, projection, phases, centroids):
    features = featurize(embeddings, projection, phases)
    group_features = lax.all_gather(features, "cent", axis=0, tiled=True)
    sharpness = SHARP_FACTOR / math.sqrt(F)

    center_wide = centroids.astype(jnp.float32)
    center_sq = jnp.sum(center_wide * center_wide, axis=1)
    inner_part = lax.dot_general(
        group_features, centroids, (((1,), (1,)), ((), ())), preferred_element_type=jnp.float32
    )
    partial_value = 2.0 * inner_part - center_sq[None, :]
    logits = sharpness * lax.psum_scatter(partial_value, "feat", scatter_dimension=0, tiled=True)

    local_top = jnp.max(logits, axis=1)
    local_sum = jnp.sum(jnp.exp(logits - local_top[:, None]), axis=1)
    n_cent = lax.axis_size("cent")
    top_score, total = local_top, local_sum
    if n_cent & (n_cent - 1) == 0:
        bit = 1
        while bit < n_cent:
            pair = lax.ppermute(
                jnp.stack([top_score, total]), "cent", [(i, i ^ bit) for i in range(n_cent)]
            )
            merged = jnp.maximum(top_score, pair[0])
            total = total * jnp.exp(top_score - merged) + pair[1] * jnp.exp(pair[0] - merged)
            top_score = merged
            bit *= 2
    else:
        pair = jnp.stack([local_top, local_sum])
        received = [pair]
        for shift in range(1, n_cent):
            received.append(lax.ppermute(pair, "cent", [(i, (i + shift) % n_cent) for i in range(n_cent)]))
        stats = jnp.stack(received)
        top_score = jnp.max(stats[:, 0], axis=0)
        total = jnp.sum(stats[:, 1] * jnp.exp(stats[:, 0] - top_score[None, :]), axis=0)
    resp = (jnp.exp(logits - top_score[:, None]) / total[:, None]).astype(jnp.bfloat16)

    group_resp = lax.all_gather(resp, "feat", axis=0, tiled=True)
    mass_part = jnp.sum(group_resp.astype(jnp.float32), axis=0)
    n_rows = group_resp.shape[1]
    split = n_rows // 4
    width = group_features.shape[1]

    def row_contract(weights):
        return lax.dot_general(
            weights, group_features, (((0,), (0,)), ((), ())), preferred_element_type=jnp.float32
        )
    n_dp = lax.axis_size("dp")
    me = lax.axis_index("dp")
    chunk = (n_rows - split) // n_dp

    def as_rows(values):
        count = -(-values.shape[-1] // width)
        padded = jnp.pad(values, [(0, 0)] * (values.ndim - 1) + [(0, count * width - values.shape[-1])])
        return padded.reshape(values.shape[:-1] + (count, width))

    both = lax.psum(jnp.concatenate([row_contract(group_resp[:, :split]), as_rows(mass_part[:split])], axis=0), "dp")
    mass = both[split:].reshape(-1)[:split]

    pieces = jnp.concatenate(
        [row_contract(group_resp[:, split:]).reshape(n_dp, chunk, width), as_rows(mass_part[split:].reshape(n_dp, chunk))], axis=1
    )
    owned = lax.dynamic_index_in_dim(pieces, me, 0, keepdims=False)
    for shift in range(1, n_dp):
        ring = [(i, (i + shift) % n_dp) for i in range(n_dp)]
        outgoing = lax.dynamic_index_in_dim(pieces, (me + shift) % n_dp, 0, keepdims=False)
        owned = owned + lax.ppermute(outgoing, "dp", ring)
    old_owned = lax.dynamic_slice_in_dim(center_wide, split + me * chunk, chunk, 0)
    mass_owned = owned[chunk:].reshape(-1)[:chunk]
    fresh = (owned[:chunk] + PRIOR_MASS * old_owned) / (mass_owned + PRIOR_MASS)[:, None]
    block = lax.dynamic_update_slice_in_dim(jnp.zeros((n_rows, width), jnp.float32), fresh, split + me * chunk, 0)
    for shift in range(1, n_dp):
        ring = [(i, (i + shift) % n_dp) for i in range(n_dp)]
        source = (me - shift) % n_dp
        block = lax.dynamic_update_slice_in_dim(block, lax.ppermute(fresh, "dp", ring), split + source * chunk, 0)

    upper = (both[:split] + PRIOR_MASS * center_wide[:split]) / (mass + PRIOR_MASS)[:, None]
    return lax.dynamic_update_slice_in_dim(block, upper, 0, 0)


def solution(mesh):
    return jax.shard_map(
        shards,
        mesh=mesh,
        in_specs=(P(("dp", "cent"), None), P(None, "feat"), P("feat"), P("cent", "feat")),
        out_specs=P("cent", "feat"),
        check_vma=False,
    )
```

```python
import math

import jax
import jax.numpy as jnp
from jax import lax
from jax.sharding import PartitionSpec as P

F = 8192


SQRT_TWO = math.sqrt(2.0)
SHARP_FACTOR = 1.5
PRIOR_MASS = 1.0


def featurize(embeddings, projection, phases):
    projected = jnp.dot(embeddings, projection, preferred_element_type=jnp.float32)
    return (SQRT_TWO * jnp.cos(projected + phases)).astype(jnp.bfloat16)


def shards(embeddings, projection, phases, centroids):
    features = featurize(embeddings, projection, phases)
    group_features = lax.all_gather(features, "cent", axis=0, tiled=True)
    sharpness = SHARP_FACTOR / math.sqrt(F)

    center_wide = centroids.astype(jnp.float32)
    center_sq = jnp.sum(center_wide * center_wide, axis=1)
    inner_part = lax.dot_general(
        group_features, centroids, (((1,), (1,)), ((), ())), preferred_element_type=jnp.float32
    )
    partial_value = 2.0 * inner_part - center_sq[None, :]
    logits = sharpness * lax.psum_scatter(partial_value, "feat", scatter_dimension=0, tiled=True)

    local_top = jnp.max(logits, axis=1)
    local_sum = jnp.sum(jnp.exp(logits - local_top[:, None]), axis=1)
    n_cent = lax.axis_size("cent")
    top_score, total = local_top, local_sum
    if n_cent & (n_cent - 1) == 0:
        bit = 1
        while bit < n_cent:
            pair = lax.ppermute(
                jnp.stack([top_score, total]), "cent", [(i, i ^ bit) for i in range(n_cent)]
            )
            merged = jnp.maximum(top_score, pair[0])
            total = total * jnp.exp(top_score - merged) + pair[1] * jnp.exp(pair[0] - merged)
            top_score = merged
            bit *= 2
    else:
        pair = jnp.stack([local_top, local_sum])
        received = [pair]
        for shift in range(1, n_cent):
            received.append(lax.ppermute(pair, "cent", [(i, (i + shift) % n_cent) for i in range(n_cent)]))
        stats = jnp.stack(received)
        top_score = jnp.max(stats[:, 0], axis=0)
        total = jnp.sum(stats[:, 1] * jnp.exp(stats[:, 0] - top_score[None, :]), axis=0)
    resp = (jnp.exp(logits - top_score[:, None]) / total[:, None]).astype(jnp.bfloat16)

    group_resp = lax.all_gather(resp, "feat", axis=0, tiled=True)
    mass_part = jnp.sum(group_resp.astype(jnp.float32), axis=0)
    n_rows = group_resp.shape[1]
    split = n_rows // 4
    width = group_features.shape[1]

    def row_contract(weights):
        return lax.dot_general(
            weights, group_features, (((0,), (0,)), ((), ())), preferred_element_type=jnp.float32
        )
    n_dp = lax.axis_size("dp")
    me = lax.axis_index("dp")
    chunk = (n_rows - split) // n_dp

    def as_rows(values):
        count = -(-values.shape[-1] // width)
        padded = jnp.pad(values, [(0, 0)] * (values.ndim - 1) + [(0, count * width - values.shape[-1])])
        return padded.reshape(values.shape[:-1] + (count, width))

    both = lax.psum(jnp.concatenate([row_contract(group_resp[:, :split]), as_rows(mass_part[:split])], axis=0), "dp")
    mass = both[split:].reshape(-1)[:split]

    pieces = jnp.concatenate(
        [row_contract(group_resp[:, split:]).reshape(n_dp, chunk, width), as_rows(mass_part[split:].reshape(n_dp, chunk))], axis=1
    )
    half = width // 2
    to_right = [(i, (i + 1) % n_dp) for i in range(n_dp)]
    to_left = [(i, (i - 1) % n_dp) for i in range(n_dp)]

    def piece(index, cols):
        return lax.dynamic_index_in_dim(pieces, index % n_dp, 0, keepdims=False)[:, cols]

    right_cols, left_cols = slice(0, half), slice(half, width)
    moving_right = piece(me - 1, right_cols)
    moving_left = piece(me + 1, left_cols)
    for step in range(1, n_dp):
        moving_right = lax.ppermute(moving_right, "dp", to_right) + piece(me - 1 - step, right_cols)
        moving_left = lax.ppermute(moving_left, "dp", to_left) + piece(me + 1 + step, left_cols)
    owned = jnp.concatenate([moving_right, moving_left], axis=1)
    old_owned = lax.dynamic_slice_in_dim(center_wide, split + me * chunk, chunk, 0)
    mass_owned = owned[chunk:].reshape(-1)[:chunk]
    fresh = (owned[:chunk] + PRIOR_MASS * old_owned) / (mass_owned + PRIOR_MASS)[:, None]

    block = lax.dynamic_update_slice_in_dim(jnp.zeros((n_rows, width), jnp.float32), fresh, split + me * chunk, 0)
    moving_right, moving_left = fresh[:, right_cols], fresh[:, left_cols]
    for step in range(1, n_dp):
        moving_right = lax.ppermute(moving_right, "dp", to_right)
        moving_left = lax.ppermute(moving_left, "dp", to_left)
        block = lax.dynamic_update_slice(block, moving_right, (split + ((me - step) % n_dp) * chunk, 0))
        block = lax.dynamic_update_slice(block, moving_left, (split + ((me + step) % n_dp) * chunk, half))

    upper = (both[:split] + PRIOR_MASS * center_wide[:split]) / (mass + PRIOR_MASS)[:, None]
    return lax.dynamic_update_slice_in_dim(block, upper, 0, 0)


def solution(mesh):
    return jax.shard_map(
        shards,
        mesh=mesh,
        in_specs=(P(("dp", "cent"), None), P(None, "feat"), P("feat"), P("cent", "feat")),
        out_specs=P("cent", "feat"),
        check_vma=False,
    )
```

```python
import math

import jax
import jax.numpy as jnp
from jax import lax
from jax.sharding import PartitionSpec as P

F = 8192


SQRT_TWO = math.sqrt(2.0)
SHARP_FACTOR = 1.5
PRIOR_MASS = 1.0


def featurize(embeddings, projection, phases):
    projected = jnp.dot(embeddings, projection, preferred_element_type=jnp.float32)
    return (SQRT_TWO * jnp.cos(projected + phases)).astype(jnp.bfloat16)


def shards(embeddings, projection, phases, centroids):
    features = featurize(embeddings, projection, phases)
    group_features = lax.all_gather(features, "cent", axis=0, tiled=True)
    sharpness = SHARP_FACTOR / math.sqrt(F)

    center_wide = centroids.astype(jnp.float32)
    center_sq = jnp.sum(center_wide * center_wide, axis=1)
    inner_part = lax.dot_general(
        group_features, centroids, (((1,), (1,)), ((), ())), preferred_element_type=jnp.float32
    )
    partial_value = 2.0 * inner_part - center_sq[None, :]
    logits = sharpness * lax.psum_scatter(partial_value, "feat", scatter_dimension=0, tiled=True)

    local_top = jnp.max(logits, axis=1)
    local_sum = jnp.sum(jnp.exp(logits - local_top[:, None]), axis=1)
    n_cent = lax.axis_size("cent")
    top_score, total = local_top, local_sum
    if n_cent & (n_cent - 1) == 0:
        bit = 1
        while bit < n_cent:
            pair = lax.ppermute(
                jnp.stack([top_score, total]), "cent", [(i, i ^ bit) for i in range(n_cent)]
            )
            merged = jnp.maximum(top_score, pair[0])
            total = total * jnp.exp(top_score - merged) + pair[1] * jnp.exp(pair[0] - merged)
            top_score = merged
            bit *= 2
    else:
        pair = jnp.stack([local_top, local_sum])
        received = [pair]
        for shift in range(1, n_cent):
            received.append(lax.ppermute(pair, "cent", [(i, (i + shift) % n_cent) for i in range(n_cent)]))
        stats = jnp.stack(received)
        top_score = jnp.max(stats[:, 0], axis=0)
        total = jnp.sum(stats[:, 1] * jnp.exp(stats[:, 0] - top_score[None, :]), axis=0)
    resp = (jnp.exp(logits - top_score[:, None]) / total[:, None]).astype(jnp.bfloat16)

    group_resp = lax.all_gather(resp, "feat", axis=0, tiled=True)
    mass_part = jnp.sum(group_resp.astype(jnp.float32), axis=0)
    n_rows = group_resp.shape[1]
    split = 3 * n_rows // 8
    width = group_features.shape[1]

    def row_contract(weights):
        return lax.dot_general(
            weights, group_features, (((0,), (0,)), ((), ())), preferred_element_type=jnp.float32
        )
    n_dp = lax.axis_size("dp")
    me = lax.axis_index("dp")
    chunk = (n_rows - split) // n_dp

    def as_rows(values):
        count = -(-values.shape[-1] // width)
        padded = jnp.pad(values, [(0, 0)] * (values.ndim - 1) + [(0, count * width - values.shape[-1])])
        return padded.reshape(values.shape[:-1] + (count, width))

    both = lax.psum(jnp.concatenate([row_contract(group_resp[:, :split]), as_rows(mass_part[:split])], axis=0), "dp")
    mass = both[split:].reshape(-1)[:split]

    pieces = jnp.concatenate(
        [row_contract(group_resp[:, split:]).reshape(n_dp, chunk, width), as_rows(mass_part[split:].reshape(n_dp, chunk))], axis=1
    )
    half = width // 2
    to_right = [(i, (i + 1) % n_dp) for i in range(n_dp)]
    to_left = [(i, (i - 1) % n_dp) for i in range(n_dp)]

    def piece(index, cols):
        return lax.dynamic_index_in_dim(pieces, index % n_dp, 0, keepdims=False)[:, cols]

    right_cols, left_cols = slice(0, half), slice(half, width)
    moving_right = piece(me - 1, right_cols)
    moving_left = piece(me + 1, left_cols)
    for step in range(1, n_dp):
        moving_right = lax.ppermute(moving_right, "dp", to_right) + piece(me - 1 - step, right_cols)
        moving_left = lax.ppermute(moving_left, "dp", to_left) + piece(me + 1 + step, left_cols)
    owned = jnp.concatenate([moving_right, moving_left], axis=1)
    old_owned = lax.dynamic_slice_in_dim(center_wide, split + me * chunk, chunk, 0)
    mass_owned = owned[chunk:].reshape(-1)[:chunk]
    fresh = (owned[:chunk] + PRIOR_MASS * old_owned) / (mass_owned + PRIOR_MASS)[:, None]

    block = lax.dynamic_update_slice_in_dim(jnp.zeros((n_rows, width), jnp.float32), fresh, split + me * chunk, 0)
    moving_right, moving_left = fresh[:, right_cols], fresh[:, left_cols]
    for step in range(1, n_dp):
        moving_right = lax.ppermute(moving_right, "dp", to_right)
        moving_left = lax.ppermute(moving_left, "dp", to_left)
        block = lax.dynamic_update_slice(block, moving_right, (split + ((me - step) % n_dp) * chunk, 0))
        block = lax.dynamic_update_slice(block, moving_left, (split + ((me + step) % n_dp) * chunk, half))

    upper = (both[:split] + PRIOR_MASS * center_wide[:split]) / (mass + PRIOR_MASS)[:, None]
    return lax.dynamic_update_slice_in_dim(block, upper, 0, 0)


def solution(mesh):
    return jax.shard_map(
        shards,
        mesh=mesh,
        in_specs=(P(("dp", "cent"), None), P(None, "feat"), P("feat"), P("cent", "feat")),
        out_specs=P("cent", "feat"),
        check_vma=False,
    )
```

```python
import math

import jax
import jax.numpy as jnp
from jax import lax
from jax.sharding import PartitionSpec as P

F = 8192


SQRT_TWO = math.sqrt(2.0)
SHARP_FACTOR = 1.5
PRIOR_MASS = 1.0


def featurize(embeddings, projection, phases):
    projected = jnp.dot(embeddings, projection, preferred_element_type=jnp.float32)
    return (SQRT_TWO * jnp.cos(projected + phases)).astype(jnp.bfloat16)


def shards(embeddings, projection, phases, centroids):
    features = featurize(embeddings, projection, phases)
    group_features = lax.all_gather(features, "cent", axis=0, tiled=True)
    sharpness = SHARP_FACTOR / math.sqrt(F)

    center_wide = centroids.astype(jnp.float32)
    center_sq = jnp.sum(center_wide * center_wide, axis=1)
    inner_part = lax.dot_general(
        group_features, centroids, (((1,), (1,)), ((), ())), preferred_element_type=jnp.float32
    )
    partial_value = 2.0 * inner_part - center_sq[None, :]
    logits = sharpness * lax.psum_scatter(partial_value, "feat", scatter_dimension=0, tiled=True)

    local_top = jnp.max(logits, axis=1)
    local_sum = jnp.sum(jnp.exp(logits - local_top[:, None]), axis=1)
    n_cent = lax.axis_size("cent")
    top_score, total = local_top, local_sum
    if n_cent & (n_cent - 1) == 0:
        bit = 1
        while bit < n_cent:
            pair = lax.ppermute(
                jnp.stack([top_score, total]), "cent", [(i, i ^ bit) for i in range(n_cent)]
            )
            merged = jnp.maximum(top_score, pair[0])
            total = total * jnp.exp(top_score - merged) + pair[1] * jnp.exp(pair[0] - merged)
            top_score = merged
            bit *= 2
    else:
        pair = jnp.stack([local_top, local_sum])
        received = [pair]
        for shift in range(1, n_cent):
            received.append(lax.ppermute(pair, "cent", [(i, (i + shift) % n_cent) for i in range(n_cent)]))
        stats = jnp.stack(received)
        top_score = jnp.max(stats[:, 0], axis=0)
        total = jnp.sum(stats[:, 1] * jnp.exp(stats[:, 0] - top_score[None, :]), axis=0)
    resp = (jnp.exp(logits - top_score[:, None]) / total[:, None]).astype(jnp.bfloat16)

    group_resp = lax.all_gather(resp, "feat", axis=0, tiled=True)
    ones = jnp.ones((group_resp.shape[0],), group_resp.dtype)
    mass_part = lax.dot_general(ones, group_resp, (((0,), (0,)), ((), ())), preferred_element_type=jnp.float32)
    n_rows = group_resp.shape[1]
    split = n_rows // 4
    width = group_features.shape[1]

    def row_contract(weights):
        return lax.dot_general(
            weights, group_features, (((0,), (0,)), ((), ())), preferred_element_type=jnp.float32
        )
    n_dp = lax.axis_size("dp")
    me = lax.axis_index("dp")
    chunk = (n_rows - split) // n_dp

    def as_rows(values):
        count = -(-values.shape[-1] // width)
        padded = jnp.pad(values, [(0, 0)] * (values.ndim - 1) + [(0, count * width - values.shape[-1])])
        return padded.reshape(values.shape[:-1] + (count, width))

    both = lax.psum(jnp.concatenate([row_contract(group_resp[:, :split]), as_rows(mass_part[:split])], axis=0), "dp")
    mass = both[split:].reshape(-1)[:split]

    pieces = jnp.concatenate(
        [row_contract(group_resp[:, split:]).reshape(n_dp, chunk, width), as_rows(mass_part[split:].reshape(n_dp, chunk))], axis=1
    )
    half = width // 2
    to_right = [(i, (i + 1) % n_dp) for i in range(n_dp)]
    to_left = [(i, (i - 1) % n_dp) for i in range(n_dp)]

    def piece(index, cols):
        return lax.dynamic_index_in_dim(pieces, index % n_dp, 0, keepdims=False)[:, cols]

    right_cols, left_cols = slice(0, half), slice(half, width)
    moving_right = piece(me - 1, right_cols)
    moving_left = piece(me + 1, left_cols)
    for step in range(1, n_dp):
        moving_right = lax.ppermute(moving_right, "dp", to_right) + piece(me - 1 - step, right_cols)
        moving_left = lax.ppermute(moving_left, "dp", to_left) + piece(me + 1 + step, left_cols)
    owned = jnp.concatenate([moving_right, moving_left], axis=1)
    old_owned = lax.dynamic_slice_in_dim(center_wide, split + me * chunk, chunk, 0)
    mass_owned = owned[chunk:].reshape(-1)[:chunk]
    fresh = (owned[:chunk] + PRIOR_MASS * old_owned) / (mass_owned + PRIOR_MASS)[:, None]

    block = lax.dynamic_update_slice_in_dim(jnp.zeros((n_rows, width), jnp.float32), fresh, split + me * chunk, 0)
    moving_right, moving_left = fresh[:, right_cols], fresh[:, left_cols]
    for step in range(1, n_dp):
        moving_right = lax.ppermute(moving_right, "dp", to_right)
        moving_left = lax.ppermute(moving_left, "dp", to_left)
        block = lax.dynamic_update_slice(block, moving_right, (split + ((me - step) % n_dp) * chunk, 0))
        block = lax.dynamic_update_slice(block, moving_left, (split + ((me + step) % n_dp) * chunk, half))

    upper = (both[:split] + PRIOR_MASS * center_wide[:split]) / (mass + PRIOR_MASS)[:, None]
    return lax.dynamic_update_slice_in_dim(block, upper, 0, 0)


def solution(mesh):
    return jax.shard_map(
        shards,
        mesh=mesh,
        in_specs=(P(("dp", "cent"), None), P(None, "feat"), P("feat"), P("cent", "feat")),
        out_specs=P("cent", "feat"),
        check_vma=False,
    )
```

```python
import math

import jax
import jax.numpy as jnp
from jax import lax
from jax.sharding import PartitionSpec as P

F = 8192


SQRT_TWO = math.sqrt(2.0)
SHARP_FACTOR = 1.5
PRIOR_MASS = 1.0


def featurize(embeddings, projection, phases):
    projected = jnp.dot(embeddings, projection, preferred_element_type=jnp.float32)
    return (SQRT_TWO * jnp.cos(projected + phases)).astype(jnp.bfloat16)


def shards(embeddings, projection, phases, centroids):
    features = featurize(embeddings, projection, phases)
    group_features = lax.all_gather(features, "cent", axis=0, tiled=True)
    sharpness = SHARP_FACTOR / math.sqrt(F)

    center_wide = centroids.astype(jnp.float32)
    center_sq = jnp.sum(center_wide * center_wide, axis=1)
    inner_part = lax.dot_general(
        group_features, centroids, (((1,), (1,)), ((), ())), preferred_element_type=jnp.float32
    )
    partial_value = 2.0 * inner_part - center_sq[None, :]
    logits = sharpness * lax.psum_scatter(partial_value, "feat", scatter_dimension=0, tiled=True)

    local_top = jnp.max(logits, axis=1)
    local_sum = jnp.sum(jnp.exp(logits - local_top[:, None]), axis=1)
    n_cent = lax.axis_size("cent")
    top_score, total = local_top, local_sum
    if n_cent & (n_cent - 1) == 0:
        bit = 1
        while bit < n_cent:
            pair = lax.ppermute(
                jnp.stack([top_score, total]), "cent", [(i, i ^ bit) for i in range(n_cent)]
            )
            merged = jnp.maximum(top_score, pair[0])
            total = total * jnp.exp(top_score - merged) + pair[1] * jnp.exp(pair[0] - merged)
            top_score = merged
            bit *= 2
    else:
        pair = jnp.stack([local_top, local_sum])
        received = [pair]
        for shift in range(1, n_cent):
            received.append(lax.ppermute(pair, "cent", [(i, (i + shift) % n_cent) for i in range(n_cent)]))
        stats = jnp.stack(received)
        top_score = jnp.max(stats[:, 0], axis=0)
        total = jnp.sum(stats[:, 1] * jnp.exp(stats[:, 0] - top_score[None, :]), axis=0)
    resp = (jnp.exp(logits - top_score[:, None]) / total[:, None]).astype(jnp.bfloat16)

    n_feat = lax.axis_size("feat")
    me_feat = lax.axis_index("feat")
    half_k = resp.shape[1] // 2
    by_sc = lax.all_gather(resp[:, :half_k], "feat", axis=0, tiled=True)
    own = resp[:, half_k:]
    arrived = [own] + [
        lax.ppermute(own, "feat", [(i, (i + shift) % n_feat) for i in range(n_feat)]) for shift in range(1, n_feat)
    ]
    by_permute = jnp.take(jnp.stack(arrived), (me_feat - jnp.arange(n_feat)) % n_feat, axis=0).reshape(-1, own.shape[1])
    group_resp = jnp.concatenate([by_sc, by_permute], axis=1)
    mass_part = jnp.sum(group_resp.astype(jnp.float32), axis=0)
    n_rows = group_resp.shape[1]
    split = n_rows // 4
    width = group_features.shape[1]

    def row_contract(weights):
        return lax.dot_general(
            weights, group_features, (((0,), (0,)), ((), ())), preferred_element_type=jnp.float32
        )
    n_dp = lax.axis_size("dp")
    me = lax.axis_index("dp")
    chunk = (n_rows - split) // n_dp

    def as_rows(values):
        count = -(-values.shape[-1] // width)
        padded = jnp.pad(values, [(0, 0)] * (values.ndim - 1) + [(0, count * width - values.shape[-1])])
        return padded.reshape(values.shape[:-1] + (count, width))

    both = lax.psum(jnp.concatenate([row_contract(group_resp[:, :split]), as_rows(mass_part[:split])], axis=0), "dp")
    mass = both[split:].reshape(-1)[:split]

    pieces = jnp.concatenate(
        [row_contract(group_resp[:, split:]).reshape(n_dp, chunk, width), as_rows(mass_part[split:].reshape(n_dp, chunk))], axis=1
    )
    half = width // 2
    to_right = [(i, (i + 1) % n_dp) for i in range(n_dp)]
    to_left = [(i, (i - 1) % n_dp) for i in range(n_dp)]

    def piece(index, cols):
        return lax.dynamic_index_in_dim(pieces, index % n_dp, 0, keepdims=False)[:, cols]

    right_cols, left_cols = slice(0, half), slice(half, width)
    moving_right = piece(me - 1, right_cols)
    moving_left = piece(me + 1, left_cols)
    for step in range(1, n_dp):
        moving_right = lax.ppermute(moving_right, "dp", to_right) + piece(me - 1 - step, right_cols)
        moving_left = lax.ppermute(moving_left, "dp", to_left) + piece(me + 1 + step, left_cols)
    owned = jnp.concatenate([moving_right, moving_left], axis=1)
    old_owned = lax.dynamic_slice_in_dim(center_wide, split + me * chunk, chunk, 0)
    mass_owned = owned[chunk:].reshape(-1)[:chunk]
    fresh = (owned[:chunk] + PRIOR_MASS * old_owned) / (mass_owned + PRIOR_MASS)[:, None]

    block = lax.dynamic_update_slice_in_dim(jnp.zeros((n_rows, width), jnp.float32), fresh, split + me * chunk, 0)
    moving_right, moving_left = fresh[:, right_cols], fresh[:, left_cols]
    for step in range(1, n_dp):
        moving_right = lax.ppermute(moving_right, "dp", to_right)
        moving_left = lax.ppermute(moving_left, "dp", to_left)
        block = lax.dynamic_update_slice(block, moving_right, (split + ((me - step) % n_dp) * chunk, 0))
        block = lax.dynamic_update_slice(block, moving_left, (split + ((me + step) % n_dp) * chunk, half))

    upper = (both[:split] + PRIOR_MASS * center_wide[:split]) / (mass + PRIOR_MASS)[:, None]
    return lax.dynamic_update_slice_in_dim(block, upper, 0, 0)


def solution(mesh):
    return jax.shard_map(
        shards,
        mesh=mesh,
        in_specs=(P(("dp", "cent"), None), P(None, "feat"), P("feat"), P("cent", "feat")),
        out_specs=P("cent", "feat"),
        check_vma=False,
    )
```

```python
import math

import jax
import jax.numpy as jnp
from jax import lax
from jax.sharding import PartitionSpec as P

F = 8192


SQRT_TWO = math.sqrt(2.0)
SHARP_FACTOR = 1.5
PRIOR_MASS = 1.0


def featurize(embeddings, projection, phases):
    projected = jnp.dot(embeddings, projection, preferred_element_type=jnp.float32)
    return (SQRT_TWO * jnp.cos(projected + phases)).astype(jnp.bfloat16)


def shards(embeddings, projection, phases, centroids):
    features = featurize(embeddings, projection, phases)
    group_features = lax.all_gather(features, "cent", axis=0, tiled=True)
    sharpness = SHARP_FACTOR / math.sqrt(F)

    center_wide = centroids.astype(jnp.float32)
    center_sq = jnp.sum(center_wide * center_wide, axis=1)
    inner_part = lax.dot_general(
        group_features, centroids, (((1,), (1,)), ((), ())), preferred_element_type=jnp.float32
    )
    partial_value = 2.0 * inner_part - center_sq[None, :]
    logits = sharpness * lax.psum_scatter(partial_value, "feat", scatter_dimension=0, tiled=True)

    local_top = jnp.max(logits, axis=1)
    local_sum = jnp.sum(jnp.exp(logits - local_top[:, None]), axis=1)
    n_cent = lax.axis_size("cent")
    top_score, total = local_top, local_sum
    if n_cent & (n_cent - 1) == 0:
        bit = 1
        while bit < n_cent:
            pair = lax.ppermute(
                jnp.stack([top_score, total]), "cent", [(i, i ^ bit) for i in range(n_cent)]
            )
            merged = jnp.maximum(top_score, pair[0])
            total = total * jnp.exp(top_score - merged) + pair[1] * jnp.exp(pair[0] - merged)
            top_score = merged
            bit *= 2
    else:
        pair = jnp.stack([local_top, local_sum])
        received = [pair]
        for shift in range(1, n_cent):
            received.append(lax.ppermute(pair, "cent", [(i, (i + shift) % n_cent) for i in range(n_cent)]))
        stats = jnp.stack(received)
        top_score = jnp.max(stats[:, 0], axis=0)
        total = jnp.sum(stats[:, 1] * jnp.exp(stats[:, 0] - top_score[None, :]), axis=0)
    resp = (jnp.exp(logits - top_score[:, None]) / total[:, None]).astype(jnp.bfloat16)

    group_resp = lax.all_gather(resp, "feat", axis=0, tiled=True)
    mass_part = jnp.sum(group_resp.astype(jnp.float32), axis=0)
    n_rows = group_resp.shape[1]
    split = n_rows // 4
    width = group_features.shape[1]

    def row_contract(weights):
        return lax.dot_general(
            weights, group_features, (((0,), (0,)), ((), ())), preferred_element_type=jnp.float32
        )
    n_dp = lax.axis_size("dp")
    me = lax.axis_index("dp")
    chunk = (n_rows - split) // n_dp

    def as_rows(values):
        count = -(-values.shape[-1] // width)
        padded = jnp.pad(values, [(0, 0)] * (values.ndim - 1) + [(0, count * width - values.shape[-1])])
        return padded.reshape(values.shape[:-1] + (count, width))

    both = lax.psum(jnp.concatenate([row_contract(group_resp[:, :split]), as_rows(mass_part[:split])], axis=0), "dp")
    mass = both[split:].reshape(-1)[:split]

    pieces = jnp.concatenate(
        [row_contract(group_resp[:, split:]).reshape(n_dp, chunk, width), as_rows(mass_part[split:].reshape(n_dp, chunk))], axis=1
    )
    half = width // 2
    to_right = [(i, (i + 1) % n_dp) for i in range(n_dp)]
    to_left = [(i, (i - 1) % n_dp) for i in range(n_dp)]

    def piece(index, cols):
        return lax.dynamic_index_in_dim(pieces, index % n_dp, 0, keepdims=False)[:, cols]

    right_cols, left_cols = slice(0, half), slice(half, width)
    if n_dp == 4:
        def piece_at(index):
            return lax.dynamic_index_in_dim(pieces, index % n_dp, 0, keepdims=False)

        far = piece_at(me + 2)
        from_left = lax.ppermute(jnp.concatenate([piece_at(me + 1), far[:, right_cols]], axis=1), "dp", to_right)
        from_right = lax.ppermute(jnp.concatenate([piece_at(me - 1), far[:, left_cols]], axis=1), "dp", to_left)
        relayed_left = lax.ppermute(from_left[:, width:], "dp", to_right)
        relayed_right = lax.ppermute(from_right[:, width:], "dp", to_left)
        owned = (
            piece_at(me)
            + from_left[:, :width]
            + from_right[:, :width]
            + jnp.concatenate([relayed_left, relayed_right], axis=1)
        )
    else:
        moving_right = piece(me - 1, right_cols)
        moving_left = piece(me + 1, left_cols)
        for step in range(1, n_dp):
            moving_right = lax.ppermute(moving_right, "dp", to_right) + piece(me - 1 - step, right_cols)
            moving_left = lax.ppermute(moving_left, "dp", to_left) + piece(me + 1 + step, left_cols)
        owned = jnp.concatenate([moving_right, moving_left], axis=1)
    old_owned = lax.dynamic_slice_in_dim(center_wide, split + me * chunk, chunk, 0)
    mass_owned = owned[chunk:].reshape(-1)[:chunk]
    fresh = (owned[:chunk] + PRIOR_MASS * old_owned) / (mass_owned + PRIOR_MASS)[:, None]

    block = lax.dynamic_update_slice_in_dim(jnp.zeros((n_rows, width), jnp.float32), fresh, split + me * chunk, 0)
    if n_dp == 4:
        from_left = lax.ppermute(fresh, "dp", to_right)
        from_right = lax.ppermute(fresh, "dp", to_left)
        relayed_left = lax.ppermute(from_left[:, right_cols], "dp", to_right)
        relayed_right = lax.ppermute(from_right[:, left_cols], "dp", to_left)
        block = lax.dynamic_update_slice_in_dim(block, from_left, split + ((me - 1) % n_dp) * chunk, 0)
        block = lax.dynamic_update_slice_in_dim(block, from_right, split + ((me + 1) % n_dp) * chunk, 0)
        opposite = jnp.concatenate([relayed_left, relayed_right], axis=1)
        block = lax.dynamic_update_slice_in_dim(block, opposite, split + ((me + 2) % n_dp) * chunk, 0)
    else:
        moving_right, moving_left = fresh[:, right_cols], fresh[:, left_cols]
        for step in range(1, n_dp):
            moving_right = lax.ppermute(moving_right, "dp", to_right)
            moving_left = lax.ppermute(moving_left, "dp", to_left)
            block = lax.dynamic_update_slice(block, moving_right, (split + ((me - step) % n_dp) * chunk, 0))
            block = lax.dynamic_update_slice(block, moving_left, (split + ((me + step) % n_dp) * chunk, half))

    upper = (both[:split] + PRIOR_MASS * center_wide[:split]) / (mass + PRIOR_MASS)[:, None]
    return lax.dynamic_update_slice_in_dim(block, upper, 0, 0)


def solution(mesh):
    return jax.shard_map(
        shards,
        mesh=mesh,
        in_specs=(P(("dp", "cent"), None), P(None, "feat"), P("feat"), P("cent", "feat")),
        out_specs=P("cent", "feat"),
        check_vma=False,
    )
```
